256 devices in a mesh: row: 32 (over z, x), col: 8 (over y, core).
Axes of the slice: x: 4, y: 4, z: 8, core: 2. Of those that a mesh axis runs over, the one named last changes fastest.
Arguments:
- tokens: bfloat16 [1024, 8192], P('row', 'col'), may hold values from -6 to 6
- cotangent: bfloat16 [1024, 8192], P('row', 'col'), may hold values from -6 to 6
- gate_weight: bfloat16 [8192, 16384], P('col', 'row'), may hold values from -0.125 to 0.125
- up_weight: bfloat16 [8192, 16384], P('col', 'row'), may hold values from -0.125 to 0.125
- down_weight: bfloat16 [16384, 8192], P('row', 'col'), may hold values from -0.078125 to 0.078125
- gate_mask: int32 [64, 128], P('col', 'row'), may hold values 0 or 1
- up_mask: int32 [64, 128], P('col', 'row'), may hold values 0 or 1
- down_mask: int32 [128, 64], P('row', 'col'), may hold values 0 or 1
Outputs:
- layer_out: bfloat16 [1024, 8192], P('row', 'col')
- grad_tokens: bfloat16 [1024, 8192], P('row', 'col')
- grad_gate_weight: float32 [8192, 16384], P('col', 'row')
- grad_up_weight: float32 [8192, 16384], P('col', 'row')
- grad_down_weight: float32 [16384, 8192], P('row', 'col')
The draws below stay inside these ranges and needn't reach their ends.
All inputs are finite; a program needn't handle non-finite values. No bound on the sum of `gate_mask` or of `up_mask` or of `down_mask` on one device may be relied on, other than what follows from the above.
Results may differ from the reference program's by a relative error of at most 0.0049.
Values may be sent and summed in bfloat16 or wider, within the bound.
No kernel may reach another device: no remote copies, remote signals or barrier semaphores. Data moves between devices by JAX's collectives and lax.ppermute only.
A program may use at most 128 MiB of HBM per device.

```python
import jax
import jax.numpy as jnp
from jax import lax

D = 8192
FF = 16384
BLOCK = 128
TOKENS = 1024


def plant(drawn, key, smallest, largest):
    longest = drawn.shape.index(max(drawn.shape))
    spots = []
    for shift in (0, 1):
        where = [jax.random.randint(jax.random.fold_in(key, axis), (), 0, length) for axis, length in enumerate(drawn.shape)]
        where[longest] = (where[longest] + shift) % drawn.shape[longest]
        spots.append(tuple(where))
    return drawn.at[spots[0]].set(smallest).at[spots[1]].set(largest)


def block_levels(stream_key, dims, shards, low, top_value):
    loudness = 1.0
    for dim, shards_of in shards:
        heights = jax.random.uniform(jax.random.fold_in(jax.random.fold_in(stream_key, 6), dim), (shards_of,), jnp.float32, low / len(shards), top_value / len(shards))
        loudness = loudness * jnp.repeat(jnp.exp(heights), dims[dim] // shards_of).reshape((-1,) + (1,) * (len(dims) - 1 - dim))
    return loudness


def bell_draw(stream_key, shape, scale, most, cuts=(), kind=jnp.bfloat16):
    loudness = block_levels(stream_key, shape, cuts, -0.22, 0.18) if cuts else 1.0
    result = jax.random.normal(stream_key, shape, jnp.float32) * scale * loudness
    return jnp.minimum(jnp.maximum(result, -most), most).astype(kind)


def setup_inputs(seed: int = 0) -> dict:
    keys = jax.random.split(jax.random.key(seed), 9)
    tokens = bell_draw(keys[0], (TOKENS, D), 1.0, 6.0, ((0, 32), (1, 8)))
    cotangent = bell_draw(keys[1], (TOKENS, D), 1.0, 6.0, ((0, 32), (1, 8)))
    gate_weight = bell_draw(keys[2], (D, FF), (3 * D // 10) ** -0.5, 0.125, ((0, 8), (1, 32)))
    up_weight = bell_draw(keys[3], (D, FF), (3 * D // 10) ** -0.5, 0.125, ((0, 8), (1, 32)))
    down_weight = bell_draw(keys[4], (FF, D), (3 * FF // 10) ** -0.5, 0.078125, ((0, 32), (1, 8)))
    gate_mask = plant((jax.random.randint(keys[5], (D // BLOCK, FF // BLOCK), 0, 10) < 3).astype(jnp.int32), jax.random.fold_in(keys[5], 1), 0, 1)
    up_mask = plant((jax.random.randint(keys[6], (D // BLOCK, FF // BLOCK), 0, 10) < 3).astype(jnp.int32), jax.random.fold_in(keys[6], 1), 0, 1)
    down_mask = plant((jax.random.randint(keys[7], (FF // BLOCK, D // BLOCK), 0, 10) < 3).astype(jnp.int32), jax.random.fold_in(keys[7], 1), 0, 1)
    return {"tokens": tokens, "cotangent": cotangent, "gate_weight": gate_weight, "up_weight": up_weight, "down_weight": down_weight, "gate_mask": gate_mask, "up_mask": up_mask, "down_mask": down_mask}


contract_inner = (((1,), (1,)), ((), ()))
contract_outer = (((0,), (0,)), ((), ()))


def apply_pattern(weight, pattern):
    row_blocks, col_blocks = pattern.shape
    block_scale = pattern.astype(weight.dtype)
    blocks = weight.reshape(row_blocks, BLOCK, col_blocks, BLOCK) * block_scale[:, None, :, None]
    return blocks.reshape(weight.shape)


def reference(tokens, cotangent, gate_weight, up_weight, down_weight, gate_mask, up_mask, down_mask):
    masked_gate = apply_pattern(gate_weight, gate_mask)
    masked_up = apply_pattern(up_weight, up_mask)
    masked_down = apply_pattern(down_weight, down_mask)
    gate_pre = jnp.dot(tokens, masked_gate, preferred_element_type=jnp.float32)
    up_pre = jnp.dot(tokens, masked_up, preferred_element_type=jnp.float32)
    sigmoid_gate = jax.nn.sigmoid(gate_pre)
    silu_gate = gate_pre * sigmoid_gate
    hidden = (silu_gate * up_pre).astype(jnp.bfloat16)
    layer_out = jnp.dot(hidden, masked_down, preferred_element_type=jnp.float32).astype(jnp.bfloat16)
    grad_hidden = lax.dot_general(cotangent, masked_down, contract_inner, preferred_element_type=jnp.float32)
    grad_gate_pre = (grad_hidden * up_pre * sigmoid_gate * (1.0 + gate_pre * (1.0 - sigmoid_gate))).astype(jnp.bfloat16)
    grad_up_pre = (grad_hidden * silu_gate).astype(jnp.bfloat16)
    grad_tokens = lax.dot_general(grad_gate_pre, masked_gate, contract_inner, preferred_element_type=jnp.float32)
    grad_tokens = grad_tokens + lax.dot_general(grad_up_pre, masked_up, contract_inner, preferred_element_type=jnp.float32)
    grad_gate_weight = apply_pattern(lax.dot_general(tokens, grad_gate_pre, contract_outer, preferred_element_type=jnp.float32), gate_mask)
    grad_up_weight = apply_pattern(lax.dot_general(tokens, grad_up_pre, contract_outer, preferred_element_type=jnp.float32), up_mask)
    grad_down_weight = apply_pattern(lax.dot_general(hidden, cotangent, contract_outer, preferred_element_type=jnp.float32), down_mask)
    return layer_out, grad_tokens.astype(jnp.bfloat16), grad_gate_weight, grad_up_weight, grad_down_weight
```

```python
import jax
import jax.numpy as jnp
from jax import lax
from jax.sharding import PartitionSpec as P

BLOCK = 128


contract_inner = (((1,), (1,)), ((), ()))
contract_outer = (((0,), (0,)), ((), ()))


def apply_pattern(weight, pattern):
    row_blocks, col_blocks = pattern.shape
    block_scale = pattern.astype(weight.dtype)
    blocks = weight.reshape(row_blocks, BLOCK, col_blocks, BLOCK) * block_scale[:, None, :, None]
    return blocks.reshape(weight.shape)


def gather_rows(x, axis, n):
    tiled = jnp.tile(x, (n, 1))
    return lax.all_to_all(tiled, axis, 0, 0, tiled=True)


def reduce_rows(x, axis, n):
    got = lax.all_to_all(x, axis, 0, 0, tiled=True)
    rows = x.shape[0] // n
    return jnp.sum(got.reshape(n, rows, x.shape[1]), axis=0)


def shards(tokens, cotangent, gate_weight, up_weight, down_weight, gate_mask, up_mask, down_mask):
    n_row = lax.axis_size("row")
    n_col = lax.axis_size("col")
    hidden_width = gate_weight.shape[1]
    features = tokens.shape[1]
    both = gather_rows(jnp.concatenate([tokens, cotangent], axis=1), "row", n_row)
    gathered_tokens = both[:, :features]
    gathered_grads = both[:, features:]
    joint_weight = jnp.concatenate(
        [apply_pattern(gate_weight, gate_mask), apply_pattern(up_weight, up_mask)], axis=1
    )
    masked_down = apply_pattern(down_weight, down_mask)
    joint_part = jnp.dot(gathered_tokens, joint_weight, preferred_element_type=jnp.float32)
    hidden_part = lax.dot_general(
        gathered_grads, masked_down, contract_inner, preferred_element_type=jnp.float32
    )
    sums = reduce_rows(jnp.concatenate([joint_part, hidden_part], axis=1), "col", n_col)
    gate_pre = sums[:, :hidden_width]
    up_pre = sums[:, hidden_width:2 * hidden_width]
    grad_hidden = sums[:, 2 * hidden_width:]
    sigmoid_gate = jax.nn.sigmoid(gate_pre)
    silu_gate = gate_pre * sigmoid_gate
    hidden_rows = (silu_gate * up_pre).astype(jnp.bfloat16)
    grad_gate_pre = grad_hidden * up_pre * sigmoid_gate * (1.0 + gate_pre * (1.0 - sigmoid_gate))
    grad_up_pre = grad_hidden * silu_gate
    rows = jnp.concatenate(
        [hidden_rows, grad_gate_pre.astype(jnp.bfloat16), grad_up_pre.astype(jnp.bfloat16)], axis=1
    )
    full = gather_rows(rows, "col", n_col)
    hidden = full[:, :hidden_width]
    joint_grad = full[:, hidden_width:]
    output_term = jnp.dot(hidden, masked_down, preferred_element_type=jnp.float32)
    token_term = lax.dot_general(
        joint_grad, joint_weight, contract_inner, preferred_element_type=jnp.float32
    )
    outs = reduce_rows(jnp.concatenate([output_term, token_term], axis=1), "row", n_row)
    layer_out = outs[:, :features]
    grad_tokens = outs[:, features:]
    weight_grads = lax.dot_general(
        gathered_tokens, joint_grad, contract_outer, preferred_element_type=jnp.float32
    )
    grad_gate_weight = apply_pattern(weight_grads[:, :hidden_width], gate_mask)
    grad_up_weight = apply_pattern(weight_grads[:, hidden_width:], up_mask)
    grad_down_weight = apply_pattern(
        lax.dot_general(hidden, gathered_grads, contract_outer, preferred_element_type=jnp.float32),
        down_mask,
    )
    return (
        layer_out.astype(jnp.bfloat16),
        grad_tokens.astype(jnp.bfloat16),
        grad_gate_weight,
        grad_up_weight,
        grad_down_weight,
    )


def solution(mesh):
    in_specs = (
        P("row", "col"),
        P("row", "col"),
        P("col", "row"),
        P("col", "row"),
        P("row", "col"),
        P("col", "row"),
        P("col", "row"),
        P("row", "col"),
    )
    out_specs = (
        P("row", "col"),
        P("row", "col"),
        P("col", "row"),
        P("col", "row"),
        P("row", "col"),
    )
    return jax.shard_map(shards, mesh=mesh, in_specs=in_specs, out_specs=out_specs, check_vma=False)
```

```python
import jax
import jax.numpy as jnp
import numpy as np
from jax import lax
from jax.sharding import Mesh
from jax.sharding import PartitionSpec as P

BLOCK = 128
ROW = ("z", "x")
COL = ("y", "core")


contract_inner = (((1,), (1,)), ((), ()))
contract_outer = (((0,), (0,)), ((), ()))


def apply_pattern(weight, pattern):
    row_blocks, col_blocks = pattern.shape
    block_scale = pattern.astype(weight.dtype)
    blocks = weight.reshape(row_blocks, BLOCK, col_blocks, BLOCK) * block_scale[:, None, :, None]
    return blocks.reshape(weight.shape)


def gather_rows(x, axis, n):
    tiled = jnp.tile(x, (n, 1))
    return lax.all_to_all(tiled, axis, 0, 0, tiled=True)


def ring_rs(x, axis, n, d):
    c = x.shape[0] // n
    i = lax.axis_index(axis)
    chunks = x.reshape((n, c) + x.shape[1:])
    perm = [(j, (j + d) % n) for j in range(n)]
    acc = lax.dynamic_index_in_dim(chunks, (i - d) % n, 0, keepdims=False)
    for s in range(1, n):
        own = lax.dynamic_index_in_dim(chunks, (i - d * (s + 1)) % n, 0, keepdims=False)
        acc = lax.ppermute(acc, axis, perm) + own
    return acc


def row_reduce(x, nz, nx):
    rows, w = x.shape
    c = rows // (nz * nx)
    q = w // 4
    outs = []
    for j in range(4):
        p = x[:, j * q:(j + 1) * q]
        d = 1 if j % 2 == 0 else -1
        if j < 2:
            outs.append(ring_rs(ring_rs(p, "z", nz, d), "x", nx, d))
        else:
            p = p.reshape(nz, nx, c, q).transpose(1, 0, 2, 3).reshape(rows, q)
            outs.append(ring_rs(ring_rs(p, "x", nx, d), "z", nz, d))
    return jnp.concatenate(outs, axis=1)


def shards(nz, nx, ny, nc, tokens, cotangent, gate_weight, up_weight, down_weight, gate_mask, up_mask, down_mask):
    hidden_width = gate_weight.shape[1]
    features = tokens.shape[1]
    local = jnp.concatenate([tokens, cotangent], axis=1)
    both = lax.all_gather(lax.all_gather(local, "x", axis=0, tiled=True), "z", axis=0, tiled=True)
    gathered_tokens = both[:, :features]
    gathered_grads = both[:, features:]
    joint_weight = jnp.concatenate(
        [apply_pattern(gate_weight, gate_mask), apply_pattern(up_weight, up_mask)], axis=1
    )
    masked_down = apply_pattern(down_weight, down_mask)
    joint_part = jnp.dot(gathered_tokens, joint_weight, preferred_element_type=jnp.float32)
    hidden_part = lax.dot_general(
        gathered_grads, masked_down, contract_inner, preferred_element_type=jnp.float32
    )
    sums = lax.psum_scatter(
        jnp.concatenate([joint_part, hidden_part], axis=1), COL, scatter_dimension=0, tiled=True
    )
    gate_pre = sums[:, :hidden_width]
    up_pre = sums[:, hidden_width:2 * hidden_width]
    grad_hidden = sums[:, 2 * hidden_width:]
    sigmoid_gate = jax.nn.sigmoid(gate_pre)
    silu_gate = gate_pre * sigmoid_gate
    hidden_rows = (silu_gate * up_pre).astype(jnp.bfloat16)
    grad_gate_pre = grad_hidden * up_pre * sigmoid_gate * (1.0 + gate_pre * (1.0 - sigmoid_gate))
    grad_up_pre = grad_hidden * silu_gate
    rows = jnp.concatenate(
        [hidden_rows, grad_gate_pre.astype(jnp.bfloat16), grad_up_pre.astype(jnp.bfloat16)], axis=1
    )
    full = gather_rows(rows, COL, ny * nc)
    hidden = full[:, :hidden_width]
    joint_grad = full[:, hidden_width:]
    output_term = jnp.dot(hidden, masked_down, preferred_element_type=jnp.float32)
    token_term = lax.dot_general(
        joint_grad, joint_weight, contract_inner, preferred_element_type=jnp.float32
    )
    outs = row_reduce(jnp.concatenate([output_term, token_term], axis=1), nz, nx)
    layer_out = outs[:, :features]
    grad_tokens = outs[:, features:]
    weight_grads = lax.dot_general(
        gathered_tokens, joint_grad, contract_outer, preferred_element_type=jnp.float32
    )
    grad_gate_weight = apply_pattern(weight_grads[:, :hidden_width], gate_mask)
    grad_up_weight = apply_pattern(weight_grads[:, hidden_width:], up_mask)
    grad_down_weight = apply_pattern(
        lax.dot_general(hidden, gathered_grads, contract_outer, preferred_element_type=jnp.float32),
        down_mask,
    )
    return (
        layer_out.astype(jnp.bfloat16),
        grad_tokens.astype(jnp.bfloat16),
        grad_gate_weight,
        grad_up_weight,
        grad_down_weight,
    )


def physical_split(devices, coord):
    coords = [getattr(d, "coords", None) for d in devices]
    if any(c is None for c in coords):
        return None
    return len({c[coord] for c in coords})


def solution(mesh):
    n_row, n_col = mesh.shape["row"], mesh.shape["col"]
    devs = mesh.devices
    nx = physical_split(list(devs[:, 0]), 0) or 4
    nz = n_row // nx
    nc = 2
    ny = n_col // nc
    m4 = Mesh(np.asarray(devs).reshape(nz, nx, ny, nc), ("z", "x", "y", "core"))
    a, w = P(ROW, COL), P(COL, ROW)
    in_specs = (a, a, w, w, a, w, w, a)
    out_specs = (a, a, w, w, a)
    body = lambda *args: shards(nz, nx, ny, nc, *args)
    return jax.shard_map(body, mesh=m4, in_specs=in_specs, out_specs=out_specs, check_vma=False)
```

```python
import jax
import jax.numpy as jnp
import numpy as np
from jax import lax
from jax.sharding import Mesh
from jax.sharding import PartitionSpec as P

BLOCK = 128
ROW = ("z", "x")
COL = ("y", "core")


contract_inner = (((1,), (1,)), ((), ()))
contract_outer = (((0,), (0,)), ((), ()))


def apply_pattern(weight, pattern):
    row_blocks, col_blocks = pattern.shape
    block_scale = pattern.astype(weight.dtype)
    blocks = weight.reshape(row_blocks, BLOCK, col_blocks, BLOCK) * block_scale[:, None, :, None]
    return blocks.reshape(weight.shape)


def gather_rows(x, axis, n):
    tiled = jnp.tile(x, (n, 1))
    return lax.all_to_all(tiled, axis, 0, 0, tiled=True)


def ring_rs(x, axis, n, d):
    c = x.shape[0] // n
    i = lax.axis_index(axis)
    chunks = x.reshape((n, c) + x.shape[1:])
    perm = [(j, (j + d) % n) for j in range(n)]
    acc = lax.dynamic_index_in_dim(chunks, (i - d) % n, 0, keepdims=False)
    for s in range(1, n):
        own = lax.dynamic_index_in_dim(chunks, (i - d * (s + 1)) % n, 0, keepdims=False)
        acc = lax.ppermute(acc, axis, perm) + own
    return acc


def row_reduce(x, nz, nx):
    w = x.shape[1]
    q = w // 2
    outs = []
    for j, d in enumerate((1, -1)):
        p = x[:, j * q:(j + 1) * q]
        outs.append(ring_rs(ring_rs(p, "z", nz, d), "x", nx, d))
    return jnp.concatenate(outs, axis=1)


def shards(nz, nx, ny, nc, tokens, cotangent, gate_weight, up_weight, down_weight, gate_mask, up_mask, down_mask):
    halves = 2
    hidden_width = gate_weight.shape[1]
    features = tokens.shape[1]
    joint_weight = jnp.concatenate(
        [apply_pattern(gate_weight, gate_mask), apply_pattern(up_weight, up_mask)], axis=1
    )
    masked_down = apply_pattern(down_weight, down_mask)
    local = jnp.concatenate([tokens, cotangent], axis=1)
    per = local.shape[0] // halves
    all_tokens, all_grads, all_hidden, all_joint_grad, outs = [], [], [], [], []
    for h in range(halves):
        part = local[h * per:(h + 1) * per]
        both = lax.all_gather(lax.all_gather(part, "x", axis=0, tiled=True), "z", axis=0, tiled=True)
        gathered_tokens = both[:, :features]
        gathered_grads = both[:, features:]
        joint_part = jnp.dot(gathered_tokens, joint_weight, preferred_element_type=jnp.float32)
        hidden_part = lax.dot_general(
            gathered_grads, masked_down, contract_inner, preferred_element_type=jnp.float32
        )
        sums = lax.psum_scatter(
            jnp.concatenate([joint_part, hidden_part], axis=1), COL, scatter_dimension=0, tiled=True
        )
        gate_pre = sums[:, :hidden_width]
        up_pre = sums[:, hidden_width:2 * hidden_width]
        grad_hidden = sums[:, 2 * hidden_width:]
        sigmoid_gate = jax.nn.sigmoid(gate_pre)
        silu_gate = gate_pre * sigmoid_gate
        hidden_rows = (silu_gate * up_pre).astype(jnp.bfloat16)
        grad_gate_pre = grad_hidden * up_pre * sigmoid_gate * (1.0 + gate_pre * (1.0 - sigmoid_gate))
        grad_up_pre = grad_hidden * silu_gate
        rows = jnp.concatenate(
            [hidden_rows, grad_gate_pre.astype(jnp.bfloat16), grad_up_pre.astype(jnp.bfloat16)], axis=1
        )
        full = gather_rows(rows, COL, ny * nc)
        hidden = full[:, :hidden_width]
        joint_grad = full[:, hidden_width:]
        output_term = jnp.dot(hidden, masked_down, preferred_element_type=jnp.float32)
        token_term = lax.dot_general(
            joint_grad, joint_weight, contract_inner, preferred_element_type=jnp.float32
        )
        outs.append(row_reduce(jnp.concatenate([output_term, token_term], axis=1), nz, nx))
        all_tokens.append(gathered_tokens)
        all_grads.append(gathered_grads)
        all_hidden.append(hidden)
        all_joint_grad.append(joint_grad)
    outs = jnp.concatenate(outs, axis=0)
    gathered_tokens = jnp.concatenate(all_tokens, axis=0)
    gathered_grads = jnp.concatenate(all_grads, axis=0)
    hidden = jnp.concatenate(all_hidden, axis=0)
    joint_grad = jnp.concatenate(all_joint_grad, axis=0)
    layer_out = outs[:, :features]
    grad_tokens = outs[:, features:]
    weight_grads = lax.dot_general(
        gathered_tokens, joint_grad, contract_outer, preferred_element_type=jnp.float32
    )
    grad_gate_weight = apply_pattern(weight_grads[:, :hidden_width], gate_mask)
    grad_up_weight = apply_pattern(weight_grads[:, hidden_width:], up_mask)
    grad_down_weight = apply_pattern(
        lax.dot_general(hidden, gathered_grads, contract_outer, preferred_element_type=jnp.float32),
        down_mask,
    )
    return (
        layer_out.astype(jnp.bfloat16),
        grad_tokens.astype(jnp.bfloat16),
        grad_gate_weight,
        grad_up_weight,
        grad_down_weight,
    )


def physical_split(devices, coord):
    coords = [getattr(d, "coords", None) for d in devices]
    if any(c is None for c in coords):
        return None
    return len({c[coord] for c in coords})


def solution(mesh):
    n_row, n_col = mesh.shape["row"], mesh.shape["col"]
    devs = mesh.devices
    nx = physical_split(list(devs[:, 0]), 0) or 4
    nz = n_row // nx
    nc = 2
    ny = n_col // nc
    m4 = Mesh(np.asarray(devs).reshape(nz, nx, ny, nc), ("z", "x", "y", "core"))
    a, w = P(ROW, COL), P(COL, ROW)
    in_specs = (a, a, w, w, a, w, w, a)
    out_specs = (a, a, w, w, a)
    def body(*args):
        return shards(nz, nx, ny, nc, *args)

    return jax.shard_map(body, mesh=m4, in_specs=in_specs, out_specs=out_specs, check_vma=False)
```

```python
import jax
import jax.numpy as jnp
import numpy as np
from jax import lax
from jax.sharding import Mesh
from jax.sharding import PartitionSpec as P

BLOCK = 128
ROW = ("z", "x")
COL = ("y", "core")


contract_inner = (((1,), (1,)), ((), ()))
contract_outer = (((0,), (0,)), ((), ()))


def apply_pattern(weight, pattern):
    row_blocks, col_blocks = pattern.shape
    block_scale = pattern.astype(weight.dtype)
    blocks = weight.reshape(row_blocks, BLOCK, col_blocks, BLOCK) * block_scale[:, None, :, None]
    return blocks.reshape(weight.shape)


def gather_rows(x, axis, n):
    tiled = jnp.tile(x, (n, 1))
    return lax.all_to_all(tiled, axis, 0, 0, tiled=True)


def ring_rs(x, axis, n, d):
    c = x.shape[0] // n
    i = lax.axis_index(axis)
    chunks = x.reshape((n, c) + x.shape[1:])
    perm = [(j, (j + d) % n) for j in range(n)]
    acc = lax.dynamic_index_in_dim(chunks, (i - d) % n, 0, keepdims=False)
    for s in range(1, n):
        own = lax.dynamic_index_in_dim(chunks, (i - d * (s + 1)) % n, 0, keepdims=False)
        acc = lax.ppermute(acc, axis, perm) + own
    return acc


def row_reduce(x, nz, nx):
    q = x.shape[1] // 2
    outs = []
    for j, d in enumerate((1, -1)):
        p = x[:, j * q:(j + 1) * q]
        p = ring_rs(p, "z", nz, d)
        outs.append(ring_rs(p, "x", nx, d))
    return jnp.concatenate(outs, axis=1)


def shards(nz, nx, ny, nc, tokens, cotangent, gate_weight, up_weight, down_weight, gate_mask, up_mask, down_mask):
    hidden_width = gate_weight.shape[1]
    features = tokens.shape[1]
    local = jnp.concatenate([tokens, cotangent], axis=1)
    both = lax.all_gather(lax.all_gather(local, "x", axis=0, tiled=True), "z", axis=0, tiled=True)
    gathered_tokens = both[:, :features]
    gathered_grads = both[:, features:]
    joint_weight = jnp.concatenate(
        [apply_pattern(gate_weight, gate_mask), apply_pattern(up_weight, up_mask)], axis=1
    )
    masked_down = apply_pattern(down_weight, down_mask)
    joint_part = jnp.dot(gathered_tokens, joint_weight, preferred_element_type=jnp.float32)
    hidden_part = lax.dot_general(
        gathered_grads, masked_down, contract_inner, preferred_element_type=jnp.float32
    )
    sums = lax.psum_scatter(
        jnp.concatenate([joint_part, hidden_part], axis=1), COL, scatter_dimension=0, tiled=True
    )
    gate_pre = sums[:, :hidden_width]
    up_pre = sums[:, hidden_width:2 * hidden_width]
    grad_hidden = sums[:, 2 * hidden_width:]
    sigmoid_gate = jax.nn.sigmoid(gate_pre)
    silu_gate = gate_pre * sigmoid_gate
    hidden_rows = (silu_gate * up_pre).astype(jnp.bfloat16)
    grad_gate_pre = grad_hidden * up_pre * sigmoid_gate * (1.0 + gate_pre * (1.0 - sigmoid_gate))
    grad_up_pre = grad_hidden * silu_gate
    rows = jnp.concatenate(
        [hidden_rows, grad_gate_pre.astype(jnp.bfloat16), grad_up_pre.astype(jnp.bfloat16)], axis=1
    )
    full = gather_rows(rows, COL, ny * nc)
    hidden = full[:, :hidden_width]
    joint_grad = full[:, hidden_width:]
    output_term = jnp.dot(hidden, masked_down, preferred_element_type=jnp.float32)
    token_term = lax.dot_general(
        joint_grad, joint_weight, contract_inner, preferred_element_type=jnp.float32
    )
    outs = row_reduce(jnp.concatenate([output_term, token_term], axis=1), nz, nx)
    layer_out = outs[:, :features]
    grad_tokens = outs[:, features:]
    weight_grads = lax.dot_general(
        gathered_tokens, joint_grad, contract_outer, preferred_element_type=jnp.float32
    )
    grad_gate_weight = apply_pattern(weight_grads[:, :hidden_width], gate_mask)
    grad_up_weight = apply_pattern(weight_grads[:, hidden_width:], up_mask)
    grad_down_weight = apply_pattern(
        lax.dot_general(hidden, gathered_grads, contract_outer, preferred_element_type=jnp.float32),
        down_mask,
    )
    return (
        layer_out.astype(jnp.bfloat16),
        grad_tokens.astype(jnp.bfloat16),
        grad_gate_weight,
        grad_up_weight,
        grad_down_weight,
    )


def physical_split(devices, coord):
    coords = [getattr(d, "coords", None) for d in devices]
    if any(c is None for c in coords):
        return None
    return len({c[coord] for c in coords})


def solution(mesh):
    n_row, n_col = mesh.shape["row"], mesh.shape["col"]
    devs = mesh.devices
    nx = physical_split(list(devs[:, 0]), 0) or 4
    nz = n_row // nx
    nc = 2
    ny = n_col // nc
    m4 = Mesh(np.asarray(devs).reshape(nz, nx, ny, nc), ("z", "x", "y", "core"))
    a, w = P(ROW, COL), P(COL, ROW)
    in_specs = (a, a, w, w, a, w, w, a)
    out_specs = (a, a, w, w, a)
    def body(*args):
        return shards(nz, nx, ny, nc, *args)

    return jax.shard_map(body, mesh=m4, in_specs=in_specs, out_specs=out_specs, check_vma=False)
```

```python
import jax
import jax.numpy as jnp
import numpy as np
from jax import lax
from jax.sharding import Mesh
from jax.sharding import PartitionSpec as P

BLOCK = 128
ROW = ("z", "x")
COL = ("y", "core")


contract_inner = (((1,), (1,)), ((), ()))
contract_outer = (((0,), (0,)), ((), ()))


def apply_pattern(weight, pattern):
    row_blocks, col_blocks = pattern.shape
    block_scale = pattern.astype(weight.dtype)
    blocks = weight.reshape(row_blocks, BLOCK, col_blocks, BLOCK) * block_scale[:, None, :, None]
    return blocks.reshape(weight.shape)


def gather_rows(x, axis, n):
    tiled = jnp.tile(x, (n, 1))
    return lax.all_to_all(tiled, axis, 0, 0, tiled=True)


def line_rs(x, axis, n):
    c = x.shape[0] // n
    i = lax.axis_index(axis)
    chunks = x.reshape((n, c) + x.shape[1:])

    def own(k):
        return lax.dynamic_index_in_dim(chunks, k % n, 0, keepdims=False)

    total = own(i)
    for reach, d in ((n // 2, 1), (n - 1 - n // 2, -1)):
        if reach == 0:
            continue
        perm = [(j, (j + d) % n) for j in range(n)]
        acc = own(i + d * reach)
        for s in range(2, reach + 1):
            acc = lax.ppermute(acc, axis, perm) + own(i + d * (reach - s + 1))
        total = total + lax.ppermute(acc, axis, perm)
    return total


def row_reduce(x, nz, nx):
    rows, w = x.shape
    c = rows // (nz * nx)
    q = w // 2
    first = line_rs(line_rs(x[:, :q], "z", nz), "x", nx)
    p = x[:, q:].reshape(nz, nx, c, q).transpose(1, 0, 2, 3).reshape(rows, q)
    second = line_rs(line_rs(p, "x", nx), "z", nz)
    return jnp.concatenate([first, second], axis=1)


def shards(nz, nx, ny, nc, tokens, cotangent, gate_weight, up_weight, down_weight, gate_mask, up_mask, down_mask):
    hidden_width = gate_weight.shape[1]
    features = tokens.shape[1]
    local = jnp.concatenate([tokens, cotangent], axis=1)
    both = lax.all_gather(lax.all_gather(local, "x", axis=0, tiled=True), "z", axis=0, tiled=True)
    gathered_tokens = both[:, :features]
    gathered_grads = both[:, features:]
    joint_weight = jnp.concatenate(
        [apply_pattern(gate_weight, gate_mask), apply_pattern(up_weight, up_mask)], axis=1
    )
    masked_down = apply_pattern(down_weight, down_mask)
    joint_part = jnp.dot(gathered_tokens, joint_weight, preferred_element_type=jnp.float32)
    hidden_part = lax.dot_general(
        gathered_grads, masked_down, contract_inner, preferred_element_type=jnp.float32
    )
    sums = lax.psum_scatter(
        jnp.concatenate([joint_part, hidden_part], axis=1), COL, scatter_dimension=0, tiled=True
    )
    gate_pre = sums[:, :hidden_width]
    up_pre = sums[:, hidden_width:2 * hidden_width]
    grad_hidden = sums[:, 2 * hidden_width:]
    sigmoid_gate = jax.nn.sigmoid(gate_pre)
    silu_gate = gate_pre * sigmoid_gate
    hidden_rows = (silu_gate * up_pre).astype(jnp.bfloat16)
    grad_gate_pre = grad_hidden * up_pre * sigmoid_gate * (1.0 + gate_pre * (1.0 - sigmoid_gate))
    grad_up_pre = grad_hidden * silu_gate
    rows = jnp.concatenate(
        [hidden_rows, grad_gate_pre.astype(jnp.bfloat16), grad_up_pre.astype(jnp.bfloat16)], axis=1
    )
    full = gather_rows(rows, COL, ny * nc)
    hidden = full[:, :hidden_width]
    joint_grad = full[:, hidden_width:]
    output_term = jnp.dot(hidden, masked_down, preferred_element_type=jnp.float32)
    token_term = lax.dot_general(
        joint_grad, joint_weight, contract_inner, preferred_element_type=jnp.float32
    )
    outs = row_reduce(jnp.concatenate([output_term, token_term], axis=1), nz, nx)
    layer_out = outs[:, :features]
    grad_tokens = outs[:, features:]
    weight_grads = lax.dot_general(
        gathered_tokens, joint_grad, contract_outer, preferred_element_type=jnp.float32
    )
    grad_gate_weight = apply_pattern(weight_grads[:, :hidden_width], gate_mask)
    grad_up_weight = apply_pattern(weight_grads[:, hidden_width:], up_mask)
    grad_down_weight = apply_pattern(
        lax.dot_general(hidden, gathered_grads, contract_outer, preferred_element_type=jnp.float32),
        down_mask,
    )
    return (
        layer_out.astype(jnp.bfloat16),
        grad_tokens.astype(jnp.bfloat16),
        grad_gate_weight,
        grad_up_weight,
        grad_down_weight,
    )


def physical_split(devices, coord):
    coords = [getattr(d, "coords", None) for d in devices]
    if any(c is None for c in coords):
        return None
    return len({c[coord] for c in coords})


def solution(mesh):
    n_row, n_col = mesh.shape["row"], mesh.shape["col"]
    devs = mesh.devices
    nx = physical_split(list(devs[:, 0]), 0) or 4
    nz = n_row // nx
    nc = 2
    ny = n_col // nc
    m4 = Mesh(np.asarray(devs).reshape(nz, nx, ny, nc), ("z", "x", "y", "core"))
    a, w = P(ROW, COL), P(COL, ROW)
    in_specs = (a, a, w, w, a, w, w, a)
    out_specs = (a, a, w, w, a)
    body = lambda *args: shards(nz, nx, ny, nc, *args)
    return jax.shard_map(body, mesh=m4, in_specs=in_specs, out_specs=out_specs, check_vma=False)
```

```python
import jax
import jax.numpy as jnp
import numpy as np
from jax import lax
from jax.sharding import Mesh
from jax.sharding import PartitionSpec as P

BLOCK = 128
ROW = ("z", "x")
COL = ("y", "core")


contract_inner = (((1,), (1,)), ((), ()))
contract_outer = (((0,), (0,)), ((), ()))


def apply_pattern(weight, pattern):
    row_blocks, col_blocks = pattern.shape
    block_scale = pattern.astype(weight.dtype)
    blocks = weight.reshape(row_blocks, BLOCK, col_blocks, BLOCK) * block_scale[:, None, :, None]
    return blocks.reshape(weight.shape)


def gather_rows(x, axis, n):
    tiled = jnp.tile(x, (n, 1))
    return lax.all_to_all(tiled, axis, 0, 0, tiled=True)


def line_rs(x, axis, n):
    c = x.shape[0] // n
    i = lax.axis_index(axis)
    chunks = x.reshape((n, c) + x.shape[1:])

    def own(k):
        return lax.dynamic_index_in_dim(chunks, k % n, 0, keepdims=False)

    total = own(i)
    for reach, d in ((n // 2, 1), (n - 1 - n // 2, -1)):
        if reach == 0:
            continue
        perm = [(j, (j + d) % n) for j in range(n)]
        acc = own(i + d * reach)
        for s in range(2, reach + 1):
            acc = lax.ppermute(acc, axis, perm) + own(i + d * (reach - s + 1))
        total = total + lax.ppermute(acc, axis, perm)
    return total


def line_ag(x, axis, n):
    c = x.shape[0]
    i = lax.axis_index(axis)
    out = jnp.zeros((n * c,) + x.shape[1:], x.dtype)
    out = lax.dynamic_update_slice_in_dim(out, x, i * c, 0)
    for reach, d in ((n // 2, 1), (n - 1 - n // 2, -1)):
        perm = [(j, (j + d) % n) for j in range(n)]
        buf = x
        for s in range(1, reach + 1):
            buf = lax.ppermute(buf, axis, perm)
            out = lax.dynamic_update_slice_in_dim(out, buf, ((i - d * s) % n) * c, 0)
    return out


def row_reduce(x, nz, nx):
    rows, w = x.shape
    c = rows // (nz * nx)
    q = w // 2
    first = line_rs(line_rs(x[:, :q], "z", nz), "x", nx)
    p = x[:, q:].reshape(nz, nx, c, q).transpose(1, 0, 2, 3).reshape(rows, q)
    second = line_rs(line_rs(p, "x", nx), "z", nz)
    return jnp.concatenate([first, second], axis=1)


def shards(nz, nx, ny, nc, tokens, cotangent, gate_weight, up_weight, down_weight, gate_mask, up_mask, down_mask):
    hidden_width = gate_weight.shape[1]
    features = tokens.shape[1]
    local = jnp.concatenate([tokens, cotangent], axis=1)
    both = line_ag(line_ag(local, "x", nx), "z", nz)
    gathered_tokens = both[:, :features]
    gathered_grads = both[:, features:]
    joint_weight = jnp.concatenate(
        [apply_pattern(gate_weight, gate_mask), apply_pattern(up_weight, up_mask)], axis=1
    )
    masked_down = apply_pattern(down_weight, down_mask)
    joint_part = jnp.dot(gathered_tokens, joint_weight, preferred_element_type=jnp.float32)
    hidden_part = lax.dot_general(
        gathered_grads, masked_down, contract_inner, preferred_element_type=jnp.float32
    )
    sums = lax.psum_scatter(
        jnp.concatenate([joint_part, hidden_part], axis=1), COL, scatter_dimension=0, tiled=True
    )
    gate_pre = sums[:, :hidden_width]
    up_pre = sums[:, hidden_width:2 * hidden_width]
    grad_hidden = sums[:, 2 * hidden_width:]
    sigmoid_gate = jax.nn.sigmoid(gate_pre)
    silu_gate = gate_pre * sigmoid_gate
    hidden_rows = (silu_gate * up_pre).astype(jnp.bfloat16)
    grad_gate_pre = grad_hidden * up_pre * sigmoid_gate * (1.0 + gate_pre * (1.0 - sigmoid_gate))
    grad_up_pre = grad_hidden * silu_gate
    rows = jnp.concatenate(
        [hidden_rows, grad_gate_pre.astype(jnp.bfloat16), grad_up_pre.astype(jnp.bfloat16)], axis=1
    )
    full = gather_rows(rows, COL, ny * nc)
    hidden = full[:, :hidden_width]
    joint_grad = full[:, hidden_width:]
    output_term = jnp.dot(hidden, masked_down, preferred_element_type=jnp.float32)
    token_term = lax.dot_general(
        joint_grad, joint_weight, contract_inner, preferred_element_type=jnp.float32
    )
    outs = row_reduce(jnp.concatenate([output_term, token_term], axis=1), nz, nx)
    layer_out = outs[:, :features]
    grad_tokens = outs[:, features:]
    weight_grads = lax.dot_general(
        gathered_tokens, joint_grad, contract_outer, preferred_element_type=jnp.float32
    )
    grad_gate_weight = apply_pattern(weight_grads[:, :hidden_width], gate_mask)
    grad_up_weight = apply_pattern(weight_grads[:, hidden_width:], up_mask)
    grad_down_weight = apply_pattern(
        lax.dot_general(hidden, gathered_grads, contract_outer, preferred_element_type=jnp.float32),
        down_mask,
    )
    return (
        layer_out.astype(jnp.bfloat16),
        grad_tokens.astype(jnp.bfloat16),
        grad_gate_weight,
        grad_up_weight,
        grad_down_weight,
    )


def physical_split(devices, coord):
    coords = [getattr(d, "coords", None) for d in devices]
    if any(c is None for c in coords):
        return None
    return len({c[coord] for c in coords})


def solution(mesh):
    n_row, n_col = mesh.shape["row"], mesh.shape["col"]
    devs = mesh.devices
    nx = physical_split(list(devs[:, 0]), 0) or 4
    nz = n_row // nx
    nc = 2
    ny = n_col // nc
    m4 = Mesh(np.asarray(devs).reshape(nz, nx, ny, nc), ("z", "x", "y", "core"))
    a, w = P(ROW, COL), P(COL, ROW)
    in_specs = (a, a, w, w, a, w, w, a)
    out_specs = (a, a, w, w, a)
    body = lambda *args: shards(nz, nx, ny, nc, *args)
    return jax.shard_map(body, mesh=m4, in_specs=in_specs, out_specs=out_specs, check_vma=False)
```

```python
import jax
import jax.numpy as jnp
import numpy as np
from jax import lax
from jax.sharding import Mesh
from jax.sharding import PartitionSpec as P

BLOCK = 128
ROW = ("z", "x")
COL = ("y", "core")


contract_inner = (((1,), (1,)), ((), ()))
contract_outer = (((0,), (0,)), ((), ()))


def apply_pattern(weight, pattern):
    row_blocks, col_blocks = pattern.shape
    block_scale = pattern.astype(weight.dtype)
    blocks = weight.reshape(row_blocks, BLOCK, col_blocks, BLOCK) * block_scale[:, None, :, None]
    return blocks.reshape(weight.shape)


def gather_rows(x, axis, n):
    tiled = jnp.tile(x, (n, 1))
    return lax.all_to_all(tiled, axis, 0, 0, tiled=True)


def line_rs(x, axis, n):
    c = x.shape[0] // n
    i = lax.axis_index(axis)
    chunks = x.reshape((n, c) + x.shape[1:])

    def own(k):
        return lax.dynamic_index_in_dim(chunks, k % n, 0, keepdims=False)

    total = own(i)
    for reach, d in ((n // 2, 1), (n - 1 - n // 2, -1)):
        if reach == 0:
            continue
        perm = [(j, (j + d) % n) for j in range(n)]
        acc = own(i + d * reach)
        for s in range(2, reach + 1):
            acc = lax.ppermute(acc, axis, perm) + own(i + d * (reach - s + 1))
        total = total + lax.ppermute(acc, axis, perm)
    return total


def line_ag(x, axis, n):
    c = x.shape[0]
    i = lax.axis_index(axis)
    out = jnp.zeros((n * c,) + x.shape[1:], x.dtype)
    out = lax.dynamic_update_slice_in_dim(out, x, i * c, 0)
    for reach, d in ((n // 2, 1), (n - 1 - n // 2, -1)):
        perm = [(j, (j + d) % n) for j in range(n)]
        buf = x
        for s in range(1, reach + 1):
            buf = lax.ppermute(buf, axis, perm)
            out = lax.dynamic_update_slice_in_dim(out, buf, ((i - d * s) % n) * c, 0)
    return out


def direct_rs(x, axis, n):
    got = lax.all_to_all(x, axis, 0, 0, tiled=True)
    return jnp.sum(got.reshape((n, x.shape[0] // n) + x.shape[1:]), axis=0)


def row_reduce(x, nz, nx):
    rows, w = x.shape
    c = rows // (nz * nx)
    q = w // 2
    first = direct_rs(line_rs(x[:, :q], "z", nz), "x", nx)
    p = x[:, q:].reshape(nz, nx, c, q).transpose(1, 0, 2, 3).reshape(rows, q)
    second = direct_rs(line_rs(p, "x", nx), "z", nz)
    return jnp.concatenate([first, second], axis=1)


def shards(nz, nx, ny, nc, tokens, cotangent, gate_weight, up_weight, down_weight, gate_mask, up_mask, down_mask):
    hidden_width = gate_weight.shape[1]
    features = tokens.shape[1]
    local = jnp.concatenate([tokens, cotangent], axis=1)
    both = line_ag(line_ag(local, "x", nx), "z", nz)
    gathered_tokens = both[:, :features]
    gathered_grads = both[:, features:]
    joint_weight = jnp.concatenate(
        [apply_pattern(gate_weight, gate_mask), apply_pattern(up_weight, up_mask)], axis=1
    )
    masked_down = apply_pattern(down_weight, down_mask)
    joint_part = jnp.dot(gathered_tokens, joint_weight, preferred_element_type=jnp.float32)
    hidden_part = lax.dot_general(
        gathered_grads, masked_down, contract_inner, preferred_element_type=jnp.float32
    )
    sums = lax.psum_scatter(
        jnp.concatenate([joint_part, hidden_part], axis=1), COL, scatter_dimension=0, tiled=True
    )
    gate_pre = sums[:, :hidden_width]
    up_pre = sums[:, hidden_width:2 * hidden_width]
    grad_hidden = sums[:, 2 * hidden_width:]
    sigmoid_gate = jax.nn.sigmoid(gate_pre)
    silu_gate = gate_pre * sigmoid_gate
    hidden_rows = (silu_gate * up_pre).astype(jnp.bfloat16)
    grad_gate_pre = grad_hidden * up_pre * sigmoid_gate * (1.0 + gate_pre * (1.0 - sigmoid_gate))
    grad_up_pre = grad_hidden * silu_gate
    rows = jnp.concatenate(
        [hidden_rows, grad_gate_pre.astype(jnp.bfloat16), grad_up_pre.astype(jnp.bfloat16)], axis=1
    )
    full = gather_rows(rows, COL, ny * nc)
    hidden = full[:, :hidden_width]
    joint_grad = full[:, hidden_width:]
    output_term = jnp.dot(hidden, masked_down, preferred_element_type=jnp.float32)
    token_term = lax.dot_general(
        joint_grad, joint_weight, contract_inner, preferred_element_type=jnp.float32
    )
    outs = row_reduce(jnp.concatenate([output_term, token_term], axis=1), nz, nx)
    layer_out = outs[:, :features]
    grad_tokens = outs[:, features:]
    weight_grads = lax.dot_general(
        gathered_tokens, joint_grad, contract_outer, preferred_element_type=jnp.float32
    )
    grad_gate_weight = apply_pattern(weight_grads[:, :hidden_width], gate_mask)
    grad_up_weight = apply_pattern(weight_grads[:, hidden_width:], up_mask)
    grad_down_weight = apply_pattern(
        lax.dot_general(hidden, gathered_grads, contract_outer, preferred_element_type=jnp.float32),
        down_mask,
    )
    return (
        layer_out.astype(jnp.bfloat16),
        grad_tokens.astype(jnp.bfloat16),
        grad_gate_weight,
        grad_up_weight,
        grad_down_weight,
    )


def physical_split(devices, coord):
    coords = [getattr(d, "coords", None) for d in devices]
    if any(c is None for c in coords):
        return None
    return len({c[coord] for c in coords})


def solution(mesh):
    n_row, n_col = mesh.shape["row"], mesh.shape["col"]
    devs = mesh.devices
    nx = physical_split(list(devs[:, 0]), 0) or 4
    nz = n_row // nx
    nc = 2
    ny = n_col // nc
    m4 = Mesh(np.asarray(devs).reshape(nz, nx, ny, nc), ("z", "x", "y", "core"))
    a, w = P(ROW, COL), P(COL, ROW)
    in_specs = (a, a, w, w, a, w, w, a)
    out_specs = (a, a, w, w, a)
    body = lambda *args: shards(nz, nx, ny, nc, *args)
    return jax.shard_map(body, mesh=m4, in_specs=in_specs, out_specs=out_specs, check_vma=False)
```

```python
import jax
import jax.numpy as jnp
import numpy as np
from jax import lax
from jax.sharding import Mesh
from jax.sharding import PartitionSpec as P

BLOCK = 128
ROW = ("z", "x")
COL = ("y", "core")


contract_inner = (((1,), (1,)), ((), ()))
contract_outer = (((0,), (0,)), ((), ()))


def apply_pattern(weight, pattern):
    row_blocks, col_blocks = pattern.shape
    block_scale = pattern.astype(weight.dtype)
    blocks = weight.reshape(row_blocks, BLOCK, col_blocks, BLOCK) * block_scale[:, None, :, None]
    return blocks.reshape(weight.shape)


def gather_rows(x, axis, n):
    tiled = jnp.tile(x, (n, 1))
    return lax.all_to_all(tiled, axis, 0, 0, tiled=True)


def line_rs(x, axis, n):
    c = x.shape[0] // n
    i = lax.axis_index(axis)
    chunks = x.reshape((n, c) + x.shape[1:])

    def own(k):
        return lax.dynamic_index_in_dim(chunks, k % n, 0, keepdims=False)

    total = own(i)
    for reach, d in ((n // 2, 1), (n - 1 - n // 2, -1)):
        if reach == 0:
            continue
        perm = [(j, (j + d) % n) for j in range(n)]
        acc = own(i + d * reach)
        for s in range(2, reach + 1):
            acc = lax.ppermute(acc, axis, perm) + own(i + d * (reach - s + 1))
        total = total + lax.ppermute(acc, axis, perm)
    return total


def line_ag(x, axis, n):
    c = x.shape[0]
    i = lax.axis_index(axis)
    out = jnp.zeros((n * c,) + x.shape[1:], x.dtype)
    out = lax.dynamic_update_slice_in_dim(out, x, i * c, 0)
    for reach, d in ((n // 2, 1), (n - 1 - n // 2, -1)):
        perm = [(j, (j + d) % n) for j in range(n)]
        buf = x
        for s in range(1, reach + 1):
            buf = lax.ppermute(buf, axis, perm)
            out = lax.dynamic_update_slice_in_dim(out, buf, ((i - d * s) % n) * c, 0)
    return out


def row_reduce(x, nz, nx):
    rows, w = x.shape
    c = rows // (nz * nx)
    q = w // 2
    first = line_rs(line_rs(x[:, :q], "z", nz), "x", nx)
    p = x[:, q:].reshape(nz, nx, c, q).transpose(1, 0, 2, 3).reshape(rows, q)
    second = line_rs(line_rs(p, "x", nx), "z", nz)
    return jnp.concatenate([first, second], axis=1)


def shards(nz, nx, ny, nc, tokens, cotangent, gate_weight, up_weight, down_weight, gate_mask, up_mask, down_mask):
    hidden_width = gate_weight.shape[1]
    features = tokens.shape[1]
    local = jnp.concatenate([tokens, cotangent], axis=1)
    both = line_ag(line_ag(local, "x", nx), "z", nz)
    gathered_tokens = both[:, :features]
    gathered_grads = both[:, features:]
    joint_weight = jnp.concatenate(
        [apply_pattern(gate_weight, gate_mask), apply_pattern(up_weight, up_mask)], axis=1
    )
    masked_down = apply_pattern(down_weight, down_mask)
    joint_part = jnp.dot(gathered_tokens, joint_weight, preferred_element_type=jnp.float32)
    hidden_part = lax.dot_general(
        gathered_grads, masked_down, contract_inner, preferred_element_type=jnp.float32
    )
    sums = lax.psum_scatter(
        jnp.concatenate([joint_part, hidden_part], axis=1), COL, scatter_dimension=0, tiled=True
    )
    gate_pre = sums[:, :hidden_width]
    up_pre = sums[:, hidden_width:2 * hidden_width]
    grad_hidden = sums[:, 2 * hidden_width:]
    sigmoid_gate = jax.nn.sigmoid(gate_pre)
    silu_gate = gate_pre * sigmoid_gate
    hidden_rows = (silu_gate * up_pre).astype(jnp.bfloat16)
    grad_gate_pre = grad_hidden * up_pre * sigmoid_gate * (1.0 + gate_pre * (1.0 - sigmoid_gate))
    grad_up_pre = grad_hidden * silu_gate
    rows = jnp.concatenate(
        [hidden_rows, grad_gate_pre.astype(jnp.bfloat16), grad_up_pre.astype(jnp.bfloat16)], axis=1
    )
    full = line_ag(line_ag(rows, "core", nc), "y", ny)
    hidden = full[:, :hidden_width]
    joint_grad = full[:, hidden_width:]
    output_term = jnp.dot(hidden, masked_down, preferred_element_type=jnp.float32)
    token_term = lax.dot_general(
        joint_grad, joint_weight, contract_inner, preferred_element_type=jnp.float32
    )
    outs = row_reduce(jnp.concatenate([output_term, token_term], axis=1), nz, nx)
    layer_out = outs[:, :features]
    grad_tokens = outs[:, features:]
    weight_grads = lax.dot_general(
        gathered_tokens, joint_grad, contract_outer, preferred_element_type=jnp.float32
    )
    grad_gate_weight = apply_pattern(weight_grads[:, :hidden_width], gate_mask)
    grad_up_weight = apply_pattern(weight_grads[:, hidden_width:], up_mask)
    grad_down_weight = apply_pattern(
        lax.dot_general(hidden, gathered_grads, contract_outer, preferred_element_type=jnp.float32),
        down_mask,
    )
    return (
        layer_out.astype(jnp.bfloat16),
        grad_tokens.astype(jnp.bfloat16),
        grad_gate_weight,
        grad_up_weight,
        grad_down_weight,
    )


def physical_split(devices, coord):
    coords = [getattr(d, "coords", None) for d in devices]
    if any(c is None for c in coords):
        return None
    return len({c[coord] for c in coords})


def solution(mesh):
    n_row, n_col = mesh.shape["row"], mesh.shape["col"]
    devs = mesh.devices
    nx = physical_split(list(devs[:, 0]), 0) or 4
    nz = n_row // nx
    nc = 2
    ny = n_col // nc
    m4 = Mesh(np.asarray(devs).reshape(nz, nx, ny, nc), ("z", "x", "y", "core"))
    a, w = P(ROW, COL), P(COL, ROW)
    in_specs = (a, a, w, w, a, w, w, a)
    out_specs = (a, a, w, w, a)
    body = lambda *args: shards(nz, nx, ny, nc, *args)
    return jax.shard_map(body, mesh=m4, in_specs=in_specs, out_specs=out_specs, check_vma=False)
```

```python
import jax
import jax.numpy as jnp
import numpy as np
from jax import lax
from jax.sharding import Mesh
from jax.sharding import PartitionSpec as P

BLOCK = 128
ROW = ("z", "x")
COL = ("y", "core")


contract_inner = (((1,), (1,)), ((), ()))
contract_outer = (((0,), (0,)), ((), ()))


def apply_pattern(weight, pattern):
    row_blocks, col_blocks = pattern.shape
    block_scale = pattern.astype(weight.dtype)
    blocks = weight.reshape(row_blocks, BLOCK, col_blocks, BLOCK) * block_scale[:, None, :, None]
    return blocks.reshape(weight.shape)


def gather_rows(x, axis, n):
    tiled = jnp.tile(x, (n, 1))
    return lax.all_to_all(tiled, axis, 0, 0, tiled=True)


def line_rs(x, axis, n, outer=1):
    c = x.shape[0] // (n * outer)
    i = lax.axis_index(axis)
    chunks = x.reshape((outer, n, c) + x.shape[1:])

    def own(k):
        part = lax.dynamic_index_in_dim(chunks, k % n, 1, keepdims=False)
        return part.reshape((outer * c,) + x.shape[1:])

    total = own(i)
    for reach, d in ((n // 2, 1), (n - 1 - n // 2, -1)):
        if reach == 0:
            continue
        perm = [(j, (j + d) % n) for j in range(n)]
        acc = own(i + d * reach)
        for s in range(2, reach + 1):
            acc = lax.ppermute(acc, axis, perm) + own(i + d * (reach - s + 1))
        total = total + lax.ppermute(acc, axis, perm)
    return total


def line_ag(x, axis, n):
    c = x.shape[0]
    i = lax.axis_index(axis)
    out = jnp.zeros((n * c,) + x.shape[1:], x.dtype)
    out = lax.dynamic_update_slice_in_dim(out, x, i * c, 0)
    for reach, d in ((n // 2, 1), (n - 1 - n // 2, -1)):
        perm = [(j, (j + d) % n) for j in range(n)]
        buf = x
        for s in range(1, reach + 1):
            buf = lax.ppermute(buf, axis, perm)
            out = lax.dynamic_update_slice_in_dim(out, buf, ((i - d * s) % n) * c, 0)
    return out


def row_reduce(x, nz, nx):
    rows, w = x.shape
    c = rows // (nz * nx)
    q = w // 2
    first = line_rs(line_rs(x[:, :q], "z", nz), "x", nx)
    second = line_rs(line_rs(x[:, q:], "x", nx, outer=nz), "z", nz)
    return jnp.concatenate([first, second], axis=1)


def shards(nz, nx, ny, nc, tokens, cotangent, gate_weight, up_weight, down_weight, gate_mask, up_mask, down_mask):
    hidden_width = gate_weight.shape[1]
    features = tokens.shape[1]
    local = jnp.concatenate([tokens, cotangent], axis=1)
    both = line_ag(line_ag(local, "x", nx), "z", nz)
    gathered_tokens = both[:, :features]
    gathered_grads = both[:, features:]
    joint_weight = jnp.concatenate(
        [apply_pattern(gate_weight, gate_mask), apply_pattern(up_weight, up_mask)], axis=1
    )
    masked_down = apply_pattern(down_weight, down_mask)
    joint_part = jnp.dot(gathered_tokens, joint_weight, preferred_element_type=jnp.float32)
    hidden_part = lax.dot_general(
        gathered_grads, masked_down, contract_inner, preferred_element_type=jnp.float32
    )
    sums = lax.psum_scatter(
        jnp.concatenate([joint_part, hidden_part], axis=1), COL, scatter_dimension=0, tiled=True
    )
    gate_pre = sums[:, :hidden_width]
    up_pre = sums[:, hidden_width:2 * hidden_width]
    grad_hidden = sums[:, 2 * hidden_width:]
    sigmoid_gate = jax.nn.sigmoid(gate_pre)
    silu_gate = gate_pre * sigmoid_gate
    hidden_rows = (silu_gate * up_pre).astype(jnp.bfloat16)
    grad_gate_pre = grad_hidden * up_pre * sigmoid_gate * (1.0 + gate_pre * (1.0 - sigmoid_gate))
    grad_up_pre = grad_hidden * silu_gate
    rows = jnp.concatenate(
        [hidden_rows, grad_gate_pre.astype(jnp.bfloat16), grad_up_pre.astype(jnp.bfloat16)], axis=1
    )
    full = line_ag(line_ag(rows, "core", nc), "y", ny)
    hidden = full[:, :hidden_width]
    joint_grad = full[:, hidden_width:]
    output_term = jnp.dot(hidden, masked_down, preferred_element_type=jnp.float32)
    token_term = lax.dot_general(
        joint_grad, joint_weight, contract_inner, preferred_element_type=jnp.float32
    )
    outs = row_reduce(jnp.concatenate([output_term, token_term], axis=1), nz, nx)
    layer_out = outs[:, :features]
    grad_tokens = outs[:, features:]
    weight_grads = lax.dot_general(
        gathered_tokens, joint_grad, contract_outer, preferred_element_type=jnp.float32
    )
    grad_gate_weight = apply_pattern(weight_grads[:, :hidden_width], gate_mask)
    grad_up_weight = apply_pattern(weight_grads[:, hidden_width:], up_mask)
    grad_down_weight = apply_pattern(
        lax.dot_general(hidden, gathered_grads, contract_outer, preferred_element_type=jnp.float32),
        down_mask,
    )
    return (
        layer_out.astype(jnp.bfloat16),
        grad_tokens.astype(jnp.bfloat16),
        grad_gate_weight,
        grad_up_weight,
        grad_down_weight,
    )


def physical_split(devices, coord):
    coords = [getattr(d, "coords", None) for d in devices]
    if any(c is None for c in coords):
        return None
    return len({c[coord] for c in coords})


def solution(mesh):
    n_row, n_col = mesh.shape["row"], mesh.shape["col"]
    devs = mesh.devices
    nx = physical_split(list(devs[:, 0]), 0) or 4
    nz = n_row // nx
    nc = 2
    ny = n_col // nc
    m4 = Mesh(np.asarray(devs).reshape(nz, nx, ny, nc), ("z", "x", "y", "core"))
    a, w = P(ROW, COL), P(COL, ROW)
    in_specs = (a, a, w, w, a, w, w, a)
    out_specs = (a, a, w, w, a)
    body = lambda *args: shards(nz, nx, ny, nc, *args)
    return jax.shard_map(body, mesh=m4, in_specs=in_specs, out_specs=out_specs, check_vma=False)
```
